128 devices in a mesh: req: 4 (over z), seq: 32 (over x, y, core).
Axes of the slice: x: 4, y: 4, z: 4, core: 2. Of those that a mesh axis runs over, the one named last changes fastest.
Arguments:
- short_tokens: bfloat16 [256, 4, 1024], P(('req', 'seq')), may hold values from -6 to 6
- long_tokens: bfloat16 [8, 4, 1024], P('req'), may hold values from -6 to 6
- short_keys: bfloat16 [256, 1024, 1024], P(('req', 'seq'))
- short_values: bfloat16 [256, 1024, 1024], P(('req', 'seq')), may hold values from -6 to 6
- long_keys: bfloat16 [8, 8192, 1024], P('req', 'seq')
- long_values: bfloat16 [8, 8192, 1024], P('req', 'seq'), may hold values from -6 to 6
- short_lengths: int32 [256], P(('req', 'seq')), may hold values from 512 to 1024
- long_lengths: int32 [8], P('req'), may hold values from 4096 to 8192
- attn_gain: float32 [1024], replicated, may hold values from 0.5 to 1.5
- ffn_gain: float32 [1024], replicated, may hold values from 0.5 to 1.5
- w_query: bfloat16 [1024, 1024], P(None, 'req'), may hold values from -0.1875 to 0.1875
- w_key: bfloat16 [1024, 1024], P(None, 'req'), may hold values from -0.1875 to 0.1875
- w_value: bfloat16 [1024, 1024], P(None, 'req'), may hold values from -0.1875 to 0.1875
- w_out: bfloat16 [1024, 1024], P('req'), may hold values from -0.1875 to 0.1875
- w_up: bfloat16 [1024, 4096], P(None, 'req'), may hold values from -0.1875 to 0.1875
- w_down: bfloat16 [4096, 1024], P('req'), may hold values from -0.09375 to 0.09375
Outputs:
- short_hidden: bfloat16 [256, 4, 1024], P(('req', 'seq'))
- long_hidden: bfloat16 [8, 4, 1024], P('req')
- short_new_keys: bfloat16 [256, 4, 1024], P(('req', 'seq'))
- short_new_values: bfloat16 [256, 4, 1024], P(('req', 'seq'))
- long_new_keys: bfloat16 [8, 4, 1024], P('req')
- long_new_values: bfloat16 [8, 4, 1024], P('req')
The draws below stay inside these ranges and needn't reach their ends.
All inputs are finite; a program needn't handle non-finite values.
Results may differ from the reference program's by a relative error of at most 0.011.
Values may be sent and summed in bfloat16 or wider, within the bound.
No kernel may reach another device: no remote copies, remote signals or barrier semaphores. Data moves between devices by JAX's collectives and lax.ppermute only.
A program may use at most 128 MiB of HBM per device.

```python
import jax
import jax.numpy as jnp
from jax import lax

D = 1024
H = 16
HD = 64
FF = 4096
SMAX = 1024
LMAX = 8192
STEPS = 4
SHORTS = 256
LONGS = 8
N_SEQ = 32


def key_field(key, count, span):
    base = jax.random.normal(key, (count, span, D), jnp.float32)
    return base.astype(jnp.bfloat16)


def draw_short_keys(key, part):
    return key_field(key, SHORTS, SMAX)


def draw_long_keys(key, part):
    return key_field(key, LONGS, LMAX)


def draw_short_lengths(key, part):
    drawn = jax.random.randint(key, (SHORTS,), SMAX // 2, SMAX + 1)
    return jnp.where(jnp.arange(SHORTS) == 0, SMAX, drawn).astype(jnp.int32)


def draw_long_lengths(key, part):
    drawn = jax.random.randint(key, (LONGS,), LMAX // 2, LMAX + 1)
    return jnp.where(jnp.arange(LONGS) == 0, LMAX, drawn).astype(jnp.int32)


def shard_levels(rng, shape, cuts, least, largest):
    def one(position, shards_of):
        heights = jax.random.uniform(jax.random.fold_in(jax.random.fold_in(rng, 6), position), (shards_of,), jnp.float32, least / len(cuts), largest / len(cuts))
        return jnp.repeat(jnp.exp(heights), shape[position] // shards_of).reshape((-1,) + (1,) * (len(shape) - position - 1))

    level = one(*cuts[0])
    for cut in cuts[1:]:
        level = level * one(*cut)
    return level


def normal_values(own_key, shape, width, bound, cuts=(), kind=jnp.bfloat16):
    array = jax.random.normal(own_key, shape, jnp.float32) * width
    if len(cuts) > 0:
        array = shard_levels(own_key, shape, cuts, -0.22, 0.18) * array
    return jnp.clip(array, min=-bound, max=bound).astype(kind)


def setup_inputs(seed: int = 0) -> dict:
    splits = jax.random.split(jax.random.key(seed), 17)
    short_tokens = normal_values(splits[0], (SHORTS, STEPS, D), 1.0, 6.0, ((0, 128),))
    long_tokens = normal_values(splits[1], (LONGS, STEPS, D), 1.0, 6.0, ((0, 4),))
    short_keys = draw_short_keys(jax.random.fold_in(splits[16], 71), 0)
    short_values = normal_values(splits[3], (SHORTS, SMAX, D), 1.0, 6.0, ((0, 128),))
    long_keys = draw_long_keys(jax.random.fold_in(splits[16], 71), 0)
    long_values = normal_values(splits[5], (LONGS, LMAX, D), 1.0, 6.0, ((0, 4), (1, 32)))
    short_lengths = draw_short_lengths(jax.random.fold_in(splits[16], 71), 0)
    long_lengths = draw_long_lengths(jax.random.fold_in(splits[16], 71), 0)
    attn_gain = jnp.clip(1.0 + 0.1 * jax.random.normal(splits[8], (D,), jnp.float32), 0.5, 1.5)
    ffn_gain = jnp.clip(1.0 + 0.1 * jax.random.normal(splits[9], (D,), jnp.float32), 0.5, 1.5)
    w_query = normal_values(splits[10], (D, D), D ** -0.5, 0.1875, ((1, 4),))
    w_key = normal_values(splits[11], (D, D), D ** -0.5, 0.1875, ((1, 4),))
    w_value = normal_values(splits[12], (D, D), D ** -0.5, 0.1875, ((1, 4),))
    w_out = normal_values(splits[13], (D, D), D ** -0.5, 0.1875, ((0, 4),))
    w_up = normal_values(splits[14], (D, FF), D ** -0.5, 0.1875, ((1, 4),))
    w_down = normal_values(splits[15], (FF, D), FF ** -0.5, 0.09375, ((0, 4),))
    return dict(short_tokens=short_tokens, long_tokens=long_tokens, short_keys=short_keys, short_values=short_values, long_keys=long_keys, long_values=long_values, short_lengths=short_lengths, long_lengths=long_lengths, attn_gain=attn_gain, ffn_gain=ffn_gain, w_query=w_query, w_key=w_key, w_value=w_value, w_out=w_out, w_up=w_up, w_down=w_down)


masked_score = -1e+30

def layer_norm(rows, gain):
    mean = lax.optimization_barrier(jnp.mean(rows, axis=-1, keepdims=True))
    centred = rows - mean
    spread = lax.optimization_barrier(jnp.mean(centred * centred, axis=-1, keepdims=True))
    return centred * lax.rsqrt(spread + 1e-05) * gain

def partial_block(query, keys, values, valid):
    scores = jnp.einsum('hd,phd->hp', query.astype(jnp.float32), keys.astype(jnp.float32)) * 0.125
    scores = jnp.where(valid[None, :], scores, masked_score)
    peak = lax.optimization_barrier(jnp.max(scores, axis=-1))
    weights = jnp.where(valid[None, :], jnp.exp(scores - peak[:, None]), 0.0)
    total = lax.optimization_barrier(jnp.sum(weights, axis=-1))
    rounded = weights.astype(jnp.bfloat16)
    output = jnp.einsum('hp,phd->hd', rounded.astype(jnp.float32), values.astype(jnp.float32))
    return (peak, total, output)

def join(first, second):
    peak = jnp.maximum(first[0], second[0])
    scale_one = jnp.exp(first[0] - peak)
    scale_two = jnp.exp(second[0] - peak)
    total = first[1] * scale_one + second[1] * scale_two
    output = first[2] * scale_one[:, None] + second[2] * scale_two[:, None]
    return (peak, total, output)

def reference(short_tokens, long_tokens, short_keys, short_values, long_keys, long_values, short_lengths, long_lengths, attn_gain, ffn_gain, w_query, w_key, w_value, w_out, w_up, w_down):
    short_count = short_tokens.shape[0]
    rows_count = short_count + long_tokens.shape[0]
    new_keys = jnp.zeros((rows_count, STEPS, D), jnp.bfloat16)
    new_values = jnp.zeros((rows_count, STEPS, D), jnp.bfloat16)
    fresh_ids = jnp.arange(STEPS)
    block = LMAX // N_SEQ
    outputs = []
    for step in range(STEPS):
        rows = jnp.concatenate([short_tokens[:, step], long_tokens[:, step]], 0).astype(jnp.float32)
        normed = layer_norm(rows, attn_gain).astype(jnp.bfloat16)
        query = jnp.dot(normed, w_query, preferred_element_type=jnp.float32).astype(jnp.bfloat16)
        key_now = jnp.dot(normed, w_key, preferred_element_type=jnp.float32).astype(jnp.bfloat16)
        value_now = jnp.dot(normed, w_value, preferred_element_type=jnp.float32).astype(jnp.bfloat16)
        new_keys = new_keys.at[:, step].set(key_now)
        new_values = new_values.at[:, step].set(value_now)
        fresh_valid = fresh_ids <= step
        queries = query.reshape(rows_count, H, HD)
        fresh_k = new_keys.reshape(rows_count, STEPS, H, HD)
        fresh_v = new_values.reshape(rows_count, STEPS, H, HD)

        def short_one(item):
            single, keys, values, length, own_k, own_v = item
            valid = jnp.arange(SMAX) < length
            cache = partial_block(single, keys.reshape(SMAX, H, HD), values.reshape(SMAX, H, HD), valid)
            fresh = partial_block(single, own_k, own_v, fresh_valid)
            peak, total, output = join(cache, fresh)
            return output / total[:, None]

        def long_one(item):
            single, keys, values, length, own_k, own_v = item
            keys = keys.reshape(N_SEQ, block, H, HD)
            values = values.reshape(N_SEQ, block, H, HD)
            places = jnp.arange(LMAX).reshape(N_SEQ, block)
            valid = places < length
            peaks, totals, outs = jax.vmap(partial_block, in_axes=(None, 0, 0, 0))(single, keys, values, valid)
            top = lax.optimization_barrier(jnp.max(peaks, axis=0))
            scale = jnp.exp(peaks - top)
            cache = (top, lax.optimization_barrier(jnp.sum(totals * scale, axis=0)), lax.optimization_barrier(jnp.sum(outs * scale[..., None], axis=0)))
            fresh = partial_block(single, own_k, own_v, fresh_valid)
            peak, total, output = join(cache, fresh)
            return output / total[:, None]
        short_att = lax.map(short_one, (queries[:short_count], short_keys, short_values, short_lengths, fresh_k[:short_count], fresh_v[:short_count]))
        long_att = lax.map(long_one, (queries[short_count:], long_keys, long_values, long_lengths, fresh_k[short_count:], fresh_v[short_count:]))
        attended = jnp.concatenate([short_att, long_att], 0).reshape(rows_count, D).astype(jnp.bfloat16)
        mixed = rows + jnp.dot(attended, w_out, preferred_element_type=jnp.float32)
        normed_ffn = layer_norm(mixed, ffn_gain).astype(jnp.bfloat16)
        hidden = jax.nn.gelu(jnp.dot(normed_ffn, w_up, preferred_element_type=jnp.float32), approximate=False).astype(jnp.bfloat16)
        result = mixed + jnp.dot(hidden, w_down, preferred_element_type=jnp.float32)
        outputs.append(result.astype(jnp.bfloat16))
    states = jnp.stack(outputs, axis=1)
    return (states[:short_count], states[short_count:], new_keys[:short_count], new_values[:short_count], new_keys[short_count:], new_values[short_count:])
```

```python
import jax
import jax.numpy as jnp
from jax import lax
from jax.sharding import PartitionSpec as P

H = 16
HD = 64


masked_score = -1e30


def layer_norm(rows, gain):
    mean = jnp.mean(rows, axis=-1, keepdims=True)
    centred = rows - mean
    spread = jnp.mean(centred * centred, axis=-1, keepdims=True)
    return centred * lax.rsqrt(spread + 1e-05) * gain


def partial_block(query, keys, values, valid):
    scores = jnp.einsum("rthd,rphd->rhtp", query, keys, preferred_element_type=jnp.float32) * 0.125
    scores = jnp.where(valid, scores, masked_score)
    peak = jnp.max(scores, axis=-1)
    weights = jnp.where(valid, jnp.exp(scores - peak[..., None]), 0.0)
    total = jnp.sum(weights, axis=-1)
    output = jnp.einsum(
        "rhtp,rphd->rhtd", weights.astype(jnp.bfloat16), values, preferred_element_type=jnp.float32
    )
    return (peak, total, output)


def join(first, second):
    peak = jnp.maximum(first[0], second[0])
    scale_one = jnp.exp(first[0] - peak)
    scale_two = jnp.exp(second[0] - peak)
    total = first[1] * scale_one + second[1] * scale_two
    output = first[2] * scale_one[..., None] + second[2] * scale_two[..., None]
    return (peak, total, output)


def merge_long(partial_value):
    peak, total, output = partial_value
    top = lax.pmax(peak, "seq")
    scale = jnp.exp(peak - top)
    total_sum, output_sum = lax.psum((total * scale, output * scale[..., None]), "seq")
    return (top, total_sum, output_sum)


def shards(
    short_tokens,
    long_tokens,
    short_keys,
    short_values,
    long_keys,
    long_values,
    short_lengths,
    long_lengths,
    attn_gain,
    ffn_gain,
    w_query,
    w_key,
    w_value,
    w_out,
    w_up,
    w_down,
):
    short_count = short_tokens.shape[0]
    long_count = long_tokens.shape[0]
    steps = short_tokens.shape[1]
    width = short_tokens.shape[2]
    req_count = short_count + long_count
    rows_count = req_count * steps
    groups = lax.axis_size("req")
    block = long_keys.shape[1]
    anchor = lax.axis_index("seq") * block
    cache_short_k = short_keys.reshape(short_count, short_keys.shape[1], H, HD)
    cache_short_v = short_values.reshape(short_count, short_keys.shape[1], H, HD)
    cache_long_k = long_keys.reshape(long_count, block, H, HD)
    cache_long_v = long_values.reshape(long_count, block, H, HD)
    short_valid = (jnp.arange(short_keys.shape[1])[None, :] < short_lengths[:, None])[:, None, None, :]
    long_valid = ((anchor + jnp.arange(block))[None, :] < long_lengths[:, None])[:, None, None, :]
    stacked = jnp.concatenate([w_query, w_key, w_value], 1)
    local = w_query.shape[1]
    fresh_ids = jnp.arange(steps)
    fresh_valid = (fresh_ids[None, :] <= fresh_ids[:, None])[None, None, :, :]

    rows = jnp.concatenate([short_tokens, long_tokens], 0).reshape(rows_count, width).astype(jnp.float32)
    normed = layer_norm(rows, attn_gain).astype(jnp.bfloat16)
    project_spread = jnp.dot(
        lax.all_gather(normed, "req", axis=0, tiled=True),
        stacked,
        preferred_element_type=jnp.float32,
    ).astype(jnp.bfloat16)
    moved = lax.all_to_all(project_spread, "req", split_axis=0, concat_axis=1, tiled=True)
    moved = moved.reshape(rows_count, groups, 3, local)
    query = moved[:, :, 0].reshape(req_count, steps, H, HD)
    key_now = moved[:, :, 1].reshape(req_count, steps, width)
    value_now = moved[:, :, 2].reshape(req_count, steps, width)
    fresh_k = key_now.reshape(req_count, steps, H, HD)
    fresh_v = value_now.reshape(req_count, steps, H, HD)
    fresh = partial_block(query, fresh_k, fresh_v, fresh_valid)
    short_part = partial_block(query[:short_count], cache_short_k, cache_short_v, short_valid)
    long_part = merge_long(
        partial_block(query[short_count:], cache_long_k, cache_long_v, long_valid)
    )
    cache_part = jax.tree.map(
        lambda first, second: jnp.concatenate([first, second], 0), short_part, long_part
    )
    peak, total, output = join(cache_part, fresh)
    attended = output / total[..., None]
    attended = attended.transpose(0, 2, 1, 3).reshape(rows_count, width).astype(jnp.bfloat16)
    spread = lax.all_to_all(attended, "req", split_axis=1, concat_axis=0, tiled=True)
    mixed = rows + lax.psum_scatter(
        jnp.dot(spread, w_out, preferred_element_type=jnp.float32),
        "req",
        scatter_dimension=0,
        tiled=True,
    )
    normed_ffn = layer_norm(mixed, ffn_gain).astype(jnp.bfloat16)
    hidden = jax.nn.gelu(
        jnp.dot(
            lax.all_gather(normed_ffn, "req", axis=0, tiled=True),
            w_up,
            preferred_element_type=jnp.float32,
        ),
        approximate=False,
    ).astype(jnp.bfloat16)
    result = mixed + lax.psum_scatter(
        jnp.dot(hidden, w_down, preferred_element_type=jnp.float32),
        "req",
        scatter_dimension=0,
        tiled=True,
    )
    states = result.astype(jnp.bfloat16).reshape(req_count, steps, width)
    return (
        states[:short_count],
        states[short_count:],
        key_now[:short_count],
        value_now[:short_count],
        key_now[short_count:],
        value_now[short_count:],
    )


def solution(mesh):
    in_specs = (
        P(("req", "seq"), None, None),
        P("req", None, None),
        P(("req", "seq"), None, None),
        P(("req", "seq"), None, None),
        P("req", "seq", None),
        P("req", "seq", None),
        P(("req", "seq")),
        P("req"),
        P(),
        P(),
        P(None, "req"),
        P(None, "req"),
        P(None, "req"),
        P("req", None),
        P(None, "req"),
        P("req", None),
    )
    out_specs = (
        P(("req", "seq"), None, None),
        P("req", None, None),
        P(("req", "seq"), None, None),
        P(("req", "seq"), None, None),
        P("req", None, None),
        P("req", None, None),
    )
    return jax.shard_map(shards, mesh=mesh, in_specs=in_specs, out_specs=out_specs, check_vma=False)
```

```python
import jax
import jax.numpy as jnp
from jax import lax
from jax.sharding import PartitionSpec as P

H = 16
HD = 64


masked_score = -1e30


def layer_norm(rows, gain):
    mean = jnp.mean(rows, axis=-1, keepdims=True)
    centred = rows - mean
    spread = jnp.mean(centred * centred, axis=-1, keepdims=True)
    return centred * lax.rsqrt(spread + 1e-05) * gain


def partial_block(query, keys, values, valid):
    scores = jnp.einsum("rthd,rphd->rhtp", query, keys, preferred_element_type=jnp.float32) * 0.125
    scores = jnp.where(valid, scores, masked_score)
    peak = jnp.max(scores, axis=-1)
    weights = jnp.where(valid, jnp.exp(scores - peak[..., None]), 0.0)
    total = jnp.sum(weights, axis=-1)
    output = jnp.einsum(
        "rhtp,rphd->rhtd", weights.astype(jnp.bfloat16), values, preferred_element_type=jnp.float32
    )
    return (peak, total, output)


def join(first, second):
    peak = jnp.maximum(first[0], second[0])
    scale_one = jnp.exp(first[0] - peak)
    scale_two = jnp.exp(second[0] - peak)
    total = first[1] * scale_one + second[1] * scale_two
    output = first[2] * scale_one[..., None] + second[2] * scale_two[..., None]
    return (peak, total, output)


def merge_long(partial_value):
    peak, total, output = partial_value
    packed = jnp.concatenate([output, peak[..., None], total[..., None]], -1)
    size = lax.axis_size("seq")
    me = lax.axis_index("seq")
    width = output.shape[-1]
    distance = 1
    while distance < size:
        pairs = [(i, i ^ distance) for i in range(size)]
        other = lax.ppermute(packed, "seq", pairs)
        lower = (me & distance) == 0
        first = jnp.where(lower, packed, other)
        second = jnp.where(lower, other, packed)
        top = jnp.maximum(first[..., width], second[..., width])
        scale_one = jnp.exp(first[..., width] - top)[..., None]
        scale_two = jnp.exp(second[..., width] - top)[..., None]
        merged = first[..., :width] * scale_one + second[..., :width] * scale_two
        summed = first[..., width + 1:] * scale_one + second[..., width + 1:] * scale_two
        packed = jnp.concatenate([merged, top[..., None], summed], -1)
        distance *= 2
    return (packed[..., width], packed[..., width + 1], packed[..., :width])


def shards(
    short_tokens,
    long_tokens,
    short_keys,
    short_values,
    long_keys,
    long_values,
    short_lengths,
    long_lengths,
    attn_gain,
    ffn_gain,
    w_query,
    w_key,
    w_value,
    w_out,
    w_up,
    w_down,
):
    short_count = short_tokens.shape[0]
    long_count = long_tokens.shape[0]
    steps = short_tokens.shape[1]
    width = short_tokens.shape[2]
    req_count = short_count + long_count
    rows_count = req_count * steps
    groups = lax.axis_size("req")
    block = long_keys.shape[1]
    anchor = lax.axis_index("seq") * block
    cache_short_k = short_keys.reshape(short_count, short_keys.shape[1], H, HD)
    cache_short_v = short_values.reshape(short_count, short_keys.shape[1], H, HD)
    cache_long_k = long_keys.reshape(long_count, block, H, HD)
    cache_long_v = long_values.reshape(long_count, block, H, HD)
    short_valid = (jnp.arange(short_keys.shape[1])[None, :] < short_lengths[:, None])[:, None, None, :]
    long_valid = ((anchor + jnp.arange(block))[None, :] < long_lengths[:, None])[:, None, None, :]
    stacked = jnp.concatenate([w_query, w_key, w_value], 1)
    local = w_query.shape[1]
    fresh_ids = jnp.arange(steps)
    fresh_valid = (fresh_ids[None, :] <= fresh_ids[:, None])[None, None, :, :]

    rows = jnp.concatenate([short_tokens, long_tokens], 0).reshape(rows_count, width).astype(jnp.float32)
    normed = layer_norm(rows, attn_gain).astype(jnp.bfloat16)
    project_spread = jnp.dot(
        lax.all_gather(normed, "req", axis=0, tiled=True),
        stacked,
        preferred_element_type=jnp.float32,
    ).astype(jnp.bfloat16)
    moved = lax.all_to_all(project_spread, "req", split_axis=0, concat_axis=1, tiled=True)
    moved = moved.reshape(rows_count, groups, 3, local)
    query = moved[:, :, 0].reshape(req_count, steps, H, HD)
    key_now = moved[:, :, 1].reshape(req_count, steps, width)
    value_now = moved[:, :, 2].reshape(req_count, steps, width)
    fresh_k = key_now.reshape(req_count, steps, H, HD)
    fresh_v = value_now.reshape(req_count, steps, H, HD)
    fresh = partial_block(query, fresh_k, fresh_v, fresh_valid)
    short_part = partial_block(query[:short_count], cache_short_k, cache_short_v, short_valid)
    long_part = merge_long(
        partial_block(query[short_count:], cache_long_k, cache_long_v, long_valid)
    )
    cache_part = jax.tree.map(
        lambda first, second: jnp.concatenate([first, second], 0), short_part, long_part
    )
    peak, total, output = join(cache_part, fresh)
    attended = output / total[..., None]
    attended = attended.transpose(0, 2, 1, 3).reshape(rows_count, width).astype(jnp.bfloat16)
    spread = lax.all_to_all(attended, "req", split_axis=1, concat_axis=0, tiled=True)
    mixed = rows + lax.psum_scatter(
        jnp.dot(spread, w_out, preferred_element_type=jnp.float32),
        "req",
        scatter_dimension=0,
        tiled=True,
    )
    normed_ffn = layer_norm(mixed, ffn_gain).astype(jnp.bfloat16)
    hidden = jax.nn.gelu(
        jnp.dot(
            lax.all_gather(normed_ffn, "req", axis=0, tiled=True),
            w_up,
            preferred_element_type=jnp.float32,
        ),
        approximate=False,
    ).astype(jnp.bfloat16)
    result = mixed + lax.psum_scatter(
        jnp.dot(hidden, w_down, preferred_element_type=jnp.float32),
        "req",
        scatter_dimension=0,
        tiled=True,
    )
    states = result.astype(jnp.bfloat16).reshape(req_count, steps, width)
    return (
        states[:short_count],
        states[short_count:],
        key_now[:short_count],
        value_now[:short_count],
        key_now[short_count:],
        value_now[short_count:],
    )


def solution(mesh):
    in_specs = (
        P(("req", "seq"), None, None),
        P("req", None, None),
        P(("req", "seq"), None, None),
        P(("req", "seq"), None, None),
        P("req", "seq", None),
        P("req", "seq", None),
        P(("req", "seq")),
        P("req"),
        P(),
        P(),
        P(None, "req"),
        P(None, "req"),
        P(None, "req"),
        P("req", None),
        P(None, "req"),
        P("req", None),
    )
    out_specs = (
        P(("req", "seq"), None, None),
        P("req", None, None),
        P(("req", "seq"), None, None),
        P(("req", "seq"), None, None),
        P("req", None, None),
        P("req", None, None),
    )
    return jax.shard_map(shards, mesh=mesh, in_specs=in_specs, out_specs=out_specs, check_vma=False)
```

```python
import jax
import jax.numpy as jnp
from jax import lax
from jax.sharding import PartitionSpec as P

H = 16
HD = 64


masked_score = -1e30


def layer_norm(rows, gain):
    mean = jnp.mean(rows, axis=-1, keepdims=True)
    centred = rows - mean
    spread = jnp.mean(centred * centred, axis=-1, keepdims=True)
    return centred * lax.rsqrt(spread + 1e-05) * gain


def partial_block(query, keys, values, valid):
    scores = jnp.einsum("rthd,rphd->rthp", query, keys, preferred_element_type=jnp.float32) * 0.125
    scores = jnp.where(valid, scores, masked_score)
    peak = jnp.max(scores, axis=-1)
    weights = jnp.where(valid, jnp.exp(scores - peak[..., None]), 0.0)
    total = jnp.sum(weights, axis=-1)
    output = jnp.einsum(
        "rthp,rphd->rthd", weights.astype(jnp.bfloat16), values, preferred_element_type=jnp.float32
    )
    return (peak, total, output)


def cache_block(query, keys, values, valid):
    reqs, steps = query.shape[0], query.shape[1]
    eye = jnp.eye(H, dtype=query.dtype)
    spread = (query[:, :, :, None, :] * eye[None, None, :, :, None]).reshape(reqs, steps * H, H * HD)
    scores = jnp.einsum("rnc,rpc->rnp", spread, keys, preferred_element_type=jnp.float32) * 0.125
    scores = jnp.where(valid, scores, masked_score)
    peak = jnp.max(scores, axis=-1)
    weights = jnp.where(valid, jnp.exp(scores - peak[..., None]), 0.0)
    total = jnp.sum(weights, axis=-1)
    full = jnp.einsum(
        "rnp,rpc->rnc", weights.astype(jnp.bfloat16), values, preferred_element_type=jnp.float32
    ).reshape(reqs, steps, H, H, HD)
    output = jnp.sum(full * eye.astype(jnp.float32)[None, None, :, :, None], axis=3)
    return (peak.reshape(reqs, steps, H), total.reshape(reqs, steps, H), output)


def join(first, second):
    peak = jnp.maximum(first[0], second[0])
    scale_one = jnp.exp(first[0] - peak)
    scale_two = jnp.exp(second[0] - peak)
    total = first[1] * scale_one + second[1] * scale_two
    output = first[2] * scale_one[..., None] + second[2] * scale_two[..., None]
    return (peak, total, output)


def merge_long(partial_value):
    peak, total, output = partial_value
    packed = jnp.concatenate([output, peak[..., None], total[..., None]], -1)
    size = lax.axis_size("seq")
    me = lax.axis_index("seq")
    width = output.shape[-1]
    distance = 1
    while distance < size:
        pairs = [(i, i ^ distance) for i in range(size)]
        other = lax.ppermute(packed, "seq", pairs)
        lower = (me & distance) == 0
        first = jnp.where(lower, packed, other)
        second = jnp.where(lower, other, packed)
        top = jnp.maximum(first[..., width], second[..., width])
        scale_one = jnp.exp(first[..., width] - top)[..., None]
        scale_two = jnp.exp(second[..., width] - top)[..., None]
        merged = first[..., :width] * scale_one + second[..., :width] * scale_two
        summed = first[..., width + 1:] * scale_one + second[..., width + 1:] * scale_two
        packed = jnp.concatenate([merged, top[..., None], summed], -1)
        distance *= 2
    return (packed[..., width], packed[..., width + 1], packed[..., :width])


def shards(
    short_tokens,
    long_tokens,
    short_keys,
    short_values,
    long_keys,
    long_values,
    short_lengths,
    long_lengths,
    attn_gain,
    ffn_gain,
    w_query,
    w_key,
    w_value,
    w_out,
    w_up,
    w_down,
):
    short_count = short_tokens.shape[0]
    long_count = long_tokens.shape[0]
    steps = short_tokens.shape[1]
    width = short_tokens.shape[2]
    req_count = short_count + long_count
    rows_count = req_count * steps
    groups = lax.axis_size("req")
    block = long_keys.shape[1]
    anchor = lax.axis_index("seq") * block
    short_valid = (jnp.arange(short_keys.shape[1])[None, :] < short_lengths[:, None])[:, None, :]
    long_valid = ((anchor + jnp.arange(block))[None, :] < long_lengths[:, None])[:, None, :]
    w_out_full = lax.all_gather(w_out, "req", axis=0, tiled=True)
    stacked = jnp.concatenate([w_query, w_key, w_value], 1)
    local = w_query.shape[1]
    fresh_ids = jnp.arange(steps)
    fresh_valid = (fresh_ids[None, :] <= fresh_ids[:, None])[None, :, None, :]

    rows = jnp.concatenate([short_tokens, long_tokens], 0).reshape(rows_count, width).astype(jnp.float32)
    normed = layer_norm(rows, attn_gain).astype(jnp.bfloat16)
    project_spread = jnp.dot(
        lax.all_gather(normed, "req", axis=0, tiled=True),
        stacked,
        preferred_element_type=jnp.float32,
    ).astype(jnp.bfloat16)
    moved = lax.all_to_all(project_spread, "req", split_axis=0, concat_axis=1, tiled=True)
    moved = moved.reshape(rows_count, groups, 3, local)
    query = moved[:, :, 0].reshape(req_count, steps, H, HD)
    key_now = moved[:, :, 1].reshape(req_count, steps, width)
    value_now = moved[:, :, 2].reshape(req_count, steps, width)
    fresh_k = key_now.reshape(req_count, steps, H, HD)
    fresh_v = value_now.reshape(req_count, steps, H, HD)
    fresh = partial_block(query, fresh_k, fresh_v, fresh_valid)
    short_part = cache_block(query[:short_count], short_keys, short_values, short_valid)
    long_part = merge_long(
        cache_block(query[short_count:], long_keys, long_values, long_valid)
    )
    cache_part = jax.tree.map(
        lambda first, second: jnp.concatenate([first, second], 0), short_part, long_part
    )
    peak, total, output = join(cache_part, fresh)
    attended = output / total[..., None]
    attended = attended.reshape(rows_count, width).astype(jnp.bfloat16)
    mixed = rows + jnp.dot(attended, w_out_full, preferred_element_type=jnp.float32)
    normed_ffn = layer_norm(mixed, ffn_gain).astype(jnp.bfloat16)
    hidden = jax.nn.gelu(
        jnp.dot(
            lax.all_gather(normed_ffn, "req", axis=0, tiled=True),
            w_up,
            preferred_element_type=jnp.float32,
        ),
        approximate=False,
    ).astype(jnp.bfloat16)
    result = mixed + lax.psum_scatter(
        jnp.dot(hidden, w_down, preferred_element_type=jnp.float32),
        "req",
        scatter_dimension=0,
        tiled=True,
    )
    states = result.astype(jnp.bfloat16).reshape(req_count, steps, width)
    return (
        states[:short_count],
        states[short_count:],
        key_now[:short_count],
        value_now[:short_count],
        key_now[short_count:],
        value_now[short_count:],
    )


def solution(mesh):
    in_specs = (
        P(("req", "seq"), None, None),
        P("req", None, None),
        P(("req", "seq"), None, None),
        P(("req", "seq"), None, None),
        P("req", "seq", None),
        P("req", "seq", None),
        P(("req", "seq")),
        P("req"),
        P(),
        P(),
        P(None, "req"),
        P(None, "req"),
        P(None, "req"),
        P("req", None),
        P(None, "req"),
        P("req", None),
    )
    out_specs = (
        P(("req", "seq"), None, None),
        P("req", None, None),
        P(("req", "seq"), None, None),
        P(("req", "seq"), None, None),
        P("req", None, None),
        P("req", None, None),
    )
    return jax.shard_map(shards, mesh=mesh, in_specs=in_specs, out_specs=out_specs, check_vma=False)
```

```python
import jax
import jax.numpy as jnp
from jax import lax
from jax.sharding import PartitionSpec as P

H = 16
HD = 64


masked_score = -1e30


def layer_norm(rows, gain):
    mean = jnp.mean(rows, axis=-1, keepdims=True)
    centred = rows - mean
    spread = jnp.mean(centred * centred, axis=-1, keepdims=True)
    return centred * lax.rsqrt(spread + 1e-05) * gain


def partial_block(query, keys, values, valid):
    scores = jnp.einsum("rthd,rphd->rthp", query, keys, preferred_element_type=jnp.float32) * 0.125
    scores = jnp.where(valid, scores, masked_score)
    peak = jnp.max(scores, axis=-1)
    weights = jnp.where(valid, jnp.exp(scores - peak[..., None]), 0.0)
    total = jnp.sum(weights, axis=-1)
    output = jnp.einsum(
        "rthp,rphd->rthd", weights.astype(jnp.bfloat16), values, preferred_element_type=jnp.float32
    )
    return (peak, total, output)


def cache_block(query, keys, values, valid):
    reqs, steps = query.shape[0], query.shape[1]
    eye = jnp.eye(H, dtype=query.dtype)
    spread = (query[:, :, :, None, :] * eye[None, None, :, :, None]).reshape(reqs, steps * H, H * HD)
    scores = jnp.einsum("rnc,rpc->rnp", spread, keys, preferred_element_type=jnp.float32) * 0.125
    scores = jnp.where(valid, scores, masked_score)
    peak = jnp.max(scores, axis=-1)
    weights = jnp.where(valid, jnp.exp(scores - peak[..., None]), 0.0)
    total = jnp.sum(weights, axis=-1)
    full = jnp.einsum(
        "rnp,rpc->rnc", weights.astype(jnp.bfloat16), values, preferred_element_type=jnp.float32
    ).reshape(reqs, steps, H, H, HD)
    output = jnp.sum(full * eye.astype(jnp.float32)[None, None, :, :, None], axis=3)
    return (peak.reshape(reqs, steps, H), total.reshape(reqs, steps, H), output)


def join(first, second):
    peak = jnp.maximum(first[0], second[0])
    scale_one = jnp.exp(first[0] - peak)
    scale_two = jnp.exp(second[0] - peak)
    total = first[1] * scale_one + second[1] * scale_two
    output = first[2] * scale_one[..., None] + second[2] * scale_two[..., None]
    return (peak, total, output)


def combine(parts, width):
    top = parts[0][..., width]
    for part in parts[1:]:
        top = jnp.maximum(top, part[..., width])
    merged = None
    summed = None
    for part in parts:
        scale = jnp.exp(part[..., width] - top)[..., None]
        out = part[..., :width] * scale
        tot = part[..., width + 1:] * scale
        merged = out if merged is None else merged + out
        summed = tot if summed is None else summed + tot
    return jnp.concatenate([merged, top[..., None], summed], -1)


def group_round(packed, size, stride, width):
    me = lax.axis_index("seq")
    total = lax.axis_size("seq")
    digit = (me // stride) % size
    received = [packed]
    for shift in range(1, size):
        pairs = []
        for i in range(total):
            e = (i // stride) % size
            pairs.append((i, i + ((e - shift) % size - e) * stride))
        received.append(lax.ppermute(packed, "seq", pairs))
    stacked = jnp.roll(jnp.stack(received), digit, axis=0)
    return combine([stacked[m] for m in range(size)], width)


def merge_long(partial_value):
    peak, total, output = partial_value
    packed = jnp.concatenate([output, peak[..., None], total[..., None]], -1)
    size = lax.axis_size("seq")
    width = output.shape[-1]
    stride = 1
    for radix in (2, 4, 4):
        if stride * radix > size or size % (stride * radix):
            break
        packed = group_round(packed, radix, stride, width)
        stride *= radix
    while stride < size:
        packed = group_round(packed, 2, stride, width)
        stride *= 2
    return (packed[..., width], packed[..., width + 1], packed[..., :width])


def req_shift(x, shift):
    n = lax.axis_size("req")
    return lax.ppermute(x, "req", [(i, (i - shift) % n) for i in range(n)])


def shards(
    short_tokens,
    long_tokens,
    short_keys,
    short_values,
    long_keys,
    long_values,
    short_lengths,
    long_lengths,
    attn_gain,
    ffn_gain,
    w_query,
    w_key,
    w_value,
    w_out,
    w_up,
    w_down,
):
    short_count = short_tokens.shape[0]
    long_count = long_tokens.shape[0]
    steps = short_tokens.shape[1]
    width = short_tokens.shape[2]
    req_count = short_count + long_count
    rows_count = req_count * steps
    groups = lax.axis_size("req")
    block = long_keys.shape[1]
    anchor = lax.axis_index("seq") * block
    short_valid = (jnp.arange(short_keys.shape[1])[None, :] < short_lengths[:, None])[:, None, :]
    long_valid = ((anchor + jnp.arange(block))[None, :] < long_lengths[:, None])[:, None, :]
    w_out_parts = jnp.concatenate(
        [w_out] + [req_shift(w_out, k) for k in range(1, lax.axis_size("req"))], 0
    )
    stacked = jnp.concatenate([w_query, w_key, w_value], 1)
    local = w_query.shape[1]
    fresh_ids = jnp.arange(steps)
    fresh_valid = (fresh_ids[None, :] <= fresh_ids[:, None])[None, :, None, :]

    rows = jnp.concatenate([short_tokens, long_tokens], 0).reshape(rows_count, width).astype(jnp.float32)
    normed = layer_norm(rows, attn_gain).astype(jnp.bfloat16)
    me = lax.axis_index("req")
    gathered = jnp.concatenate([normed] + [req_shift(normed, k) for k in range(1, groups)], 0)
    project_spread = jnp.dot(gathered, stacked, preferred_element_type=jnp.float32).astype(jnp.bfloat16)
    chunks = project_spread.reshape(groups, rows_count, 3 * local)
    returned = jnp.stack([chunks[0]] + [req_shift(chunks[groups - j], j) for j in range(1, groups)])
    moved = jnp.roll(returned, me, axis=0).transpose(1, 0, 2)
    moved = moved.reshape(rows_count, groups, 3, local)
    query = moved[:, :, 0].reshape(req_count, steps, H, HD)
    key_now = moved[:, :, 1].reshape(req_count, steps, width)
    value_now = moved[:, :, 2].reshape(req_count, steps, width)
    fresh_k = key_now.reshape(req_count, steps, H, HD)
    fresh_v = value_now.reshape(req_count, steps, H, HD)
    fresh = partial_block(query, fresh_k, fresh_v, fresh_valid)
    short_part = cache_block(query[:short_count], short_keys, short_values, short_valid)
    long_part = merge_long(
        cache_block(query[short_count:], long_keys, long_values, long_valid)
    )
    cache_part = jax.tree.map(
        lambda first, second: jnp.concatenate([first, second], 0), short_part, long_part
    )
    peak, total, output = join(cache_part, fresh)
    attended = output / total[..., None]
    attended = attended.reshape(rows_count, groups, width // groups).astype(jnp.bfloat16)
    attended = jnp.roll(attended, -me, axis=1).reshape(rows_count, width)
    mixed = rows + jnp.dot(attended, w_out_parts, preferred_element_type=jnp.float32)
    normed_ffn = layer_norm(mixed, ffn_gain).astype(jnp.bfloat16)
    gathered_ffn = jnp.concatenate(
        [normed_ffn] + [req_shift(normed_ffn, k) for k in range(1, groups)], 0
    )
    hidden = jax.nn.gelu(
        jnp.dot(gathered_ffn, w_up, preferred_element_type=jnp.float32),
        approximate=False,
    ).astype(jnp.bfloat16)
    down = jnp.dot(hidden, w_down, preferred_element_type=jnp.float32).reshape(groups, rows_count, width)
    reduced = down[0]
    for k in range(1, groups):
        reduced = reduced + req_shift(down[k], groups - k)
    result = mixed + reduced
    states = result.astype(jnp.bfloat16).reshape(req_count, steps, width)
    return (
        states[:short_count],
        states[short_count:],
        key_now[:short_count],
        value_now[:short_count],
        key_now[short_count:],
        value_now[short_count:],
    )


def solution(mesh):
    in_specs = (
        P(("req", "seq"), None, None),
        P("req", None, None),
        P(("req", "seq"), None, None),
        P(("req", "seq"), None, None),
        P("req", "seq", None),
        P("req", "seq", None),
        P(("req", "seq")),
        P("req"),
        P(),
        P(),
        P(None, "req"),
        P(None, "req"),
        P(None, "req"),
        P("req", None),
        P(None, "req"),
        P("req", None),
    )
    out_specs = (
        P(("req", "seq"), None, None),
        P("req", None, None),
        P(("req", "seq"), None, None),
        P(("req", "seq"), None, None),
        P("req", None, None),
        P("req", None, None),
    )
    return jax.shard_map(shards, mesh=mesh, in_specs=in_specs, out_specs=out_specs, check_vma=False)
```

```python
import jax
import jax.numpy as jnp
from jax import lax
from jax.sharding import PartitionSpec as P

H = 16
HD = 64


masked_score = -1e30


def layer_norm(rows, gain):
    mean = jnp.mean(rows, axis=-1, keepdims=True)
    centred = rows - mean
    spread = jnp.mean(centred * centred, axis=-1, keepdims=True)
    return centred * lax.rsqrt(spread + 1e-05) * gain


def partial_block(query, keys, values, valid):
    scores = jnp.einsum("rthd,rphd->rthp", query, keys, preferred_element_type=jnp.float32) * 0.125
    scores = jnp.where(valid, scores, masked_score)
    peak = jnp.max(scores, axis=-1)
    weights = jnp.where(valid, jnp.exp(scores - peak[..., None]), 0.0)
    total = jnp.sum(weights, axis=-1)
    output = jnp.einsum(
        "rthp,rphd->rthd", weights.astype(jnp.bfloat16), values, preferred_element_type=jnp.float32
    )
    return (peak, total, output)


def cache_block(query, keys, values, valid):
    reqs, steps = query.shape[0], query.shape[1]
    eye = jnp.eye(H, dtype=query.dtype)
    spread = (query[:, :, :, None, :] * eye[None, None, :, :, None]).reshape(reqs, steps * H, H * HD)
    scores = jnp.einsum("rnc,rpc->rnp", spread, keys, preferred_element_type=jnp.float32) * 0.125
    scores = jnp.where(valid, scores, masked_score)
    peak = jnp.max(scores, axis=-1)
    weights = jnp.where(valid, jnp.exp(scores - peak[..., None]), 0.0)
    total = jnp.sum(weights, axis=-1)
    full = jnp.einsum(
        "rnp,rpc->rnc", weights.astype(jnp.bfloat16), values, preferred_element_type=jnp.float32
    ).reshape(reqs, steps, H, H, HD)
    output = jnp.sum(full * eye.astype(jnp.float32)[None, None, :, :, None], axis=3)
    return (peak.reshape(reqs, steps, H), total.reshape(reqs, steps, H), output)


def join(first, second):
    peak = jnp.maximum(first[0], second[0])
    scale_one = jnp.exp(first[0] - peak)
    scale_two = jnp.exp(second[0] - peak)
    total = first[1] * scale_one + second[1] * scale_two
    output = first[2] * scale_one[..., None] + second[2] * scale_two[..., None]
    return (peak, total, output)


def combine(parts, width):
    top = parts[0][..., width]
    for part in parts[1:]:
        top = jnp.maximum(top, part[..., width])
    merged = None
    summed = None
    for part in parts:
        scale = jnp.exp(part[..., width] - top)[..., None]
        out = part[..., :width] * scale
        tot = part[..., width + 1:] * scale
        merged = out if merged is None else merged + out
        summed = tot if summed is None else summed + tot
    return jnp.concatenate([merged, top[..., None], summed], -1)


def group_round_body(packed, size, stride, width):
    me = lax.axis_index("seq")
    total = lax.axis_size("seq")
    digit = (me // stride) % size
    received = [packed]
    for shift in range(1, size):
        pairs = []
        for i in range(total):
            e = (i // stride) % size
            pairs.append((i, i + ((e - shift) % size - e) * stride))
        received.append(lax.ppermute(packed, "seq", pairs))
    stacked = jnp.roll(jnp.stack(received), digit, axis=0)
    return combine([stacked[m] for m in range(size)], width)


def merge_long(partial_value):
    peak, total, output = partial_value
    packed = jnp.concatenate([output, peak[..., None], total[..., None]], -1)
    size = lax.axis_size("seq")
    width = output.shape[-1]
    stride = 1
    for radix in (2, 4, 4):
        if stride * radix > size or size % (stride * radix):
            break
        packed = group_round_body(packed, radix, stride, width)
        stride *= radix
    while stride < size:
        packed = group_round_body(packed, 2, stride, width)
        stride *= 2
    return (packed[..., width], packed[..., width + 1], packed[..., :width])


def req_shift(x, shift):
    n = lax.axis_size("req")
    return lax.ppermute(x, "req", [(i, (i - shift) % n) for i in range(n)])


def shards(
    short_tokens,
    long_tokens,
    short_keys,
    short_values,
    long_keys,
    long_values,
    short_lengths,
    long_lengths,
    attn_gain,
    ffn_gain,
    w_query,
    w_key,
    w_value,
    w_out,
    w_up,
    w_down,
):
    short_count = short_tokens.shape[0]
    long_count = long_tokens.shape[0]
    steps = short_tokens.shape[1]
    width = short_tokens.shape[2]
    req_count = short_count + long_count
    rows_count = req_count * steps
    groups = lax.axis_size("req")
    block = long_keys.shape[1]
    anchor = lax.axis_index("seq") * block
    short_valid = (jnp.arange(short_keys.shape[1])[None, :] < short_lengths[:, None])[:, None, :]
    long_valid = ((anchor + jnp.arange(block))[None, :] < long_lengths[:, None])[:, None, :]
    stacked = jnp.concatenate([w_query, w_key, w_value], 1)
    local = w_query.shape[1]
    fresh_ids = jnp.arange(steps)
    fresh_valid = (fresh_ids[None, :] <= fresh_ids[:, None])[None, :, None, :]

    rows = jnp.concatenate([short_tokens, long_tokens], 0).reshape(rows_count, width).astype(jnp.float32)
    normed = layer_norm(rows, attn_gain).astype(jnp.bfloat16)
    me = lax.axis_index("req")
    gathered = jnp.concatenate([normed] + [req_shift(normed, k) for k in range(1, groups)], 0)
    project_spread = jnp.dot(gathered, stacked, preferred_element_type=jnp.float32).astype(jnp.bfloat16)
    chunks = project_spread.reshape(groups, rows_count, 3 * local)
    returned = jnp.stack([chunks[0]] + [req_shift(chunks[groups - j], j) for j in range(1, groups)])
    moved = jnp.roll(returned, me, axis=0).transpose(1, 0, 2)
    moved = moved.reshape(rows_count, groups, 3, local)
    w_out, moved = lax.optimization_barrier((w_out, moved))
    w_out_parts = jnp.concatenate(
        [w_out] + [req_shift(w_out, k) for k in range(1, groups)], 0
    )
    query = moved[:, :, 0].reshape(req_count, steps, H, HD)
    key_now = moved[:, :, 1].reshape(req_count, steps, width)
    value_now = moved[:, :, 2].reshape(req_count, steps, width)
    fresh_k = key_now.reshape(req_count, steps, H, HD)
    fresh_v = value_now.reshape(req_count, steps, H, HD)
    long_raw = cache_block(query[short_count:], long_keys, long_values, long_valid)
    long_raw, query, fresh_k, fresh_v = lax.optimization_barrier((long_raw, query, fresh_k, fresh_v))
    long_part = merge_long(long_raw)
    fresh = partial_block(query, fresh_k, fresh_v, fresh_valid)
    short_part = cache_block(query[:short_count], short_keys, short_values, short_valid)
    cache_part = jax.tree.map(
        lambda first, second: jnp.concatenate([first, second], 0), short_part, long_part
    )
    _, total, output = join(cache_part, fresh)
    attended = output / total[..., None]
    attended = attended.reshape(rows_count, groups, width // groups).astype(jnp.bfloat16)
    attended = jnp.roll(attended, -me, axis=1).reshape(rows_count, width)
    mixed = rows + jnp.dot(attended, w_out_parts, preferred_element_type=jnp.float32)
    normed_ffn = layer_norm(mixed, ffn_gain).astype(jnp.bfloat16)
    gathered_ffn = jnp.concatenate(
        [normed_ffn] + [req_shift(normed_ffn, k) for k in range(1, groups)], 0
    )
    hidden = jax.nn.gelu(
        jnp.dot(gathered_ffn, w_up, preferred_element_type=jnp.float32),
        approximate=False,
    ).astype(jnp.bfloat16)
    down = jnp.dot(hidden, w_down, preferred_element_type=jnp.float32).reshape(groups, rows_count, width)
    reduced = down[0]
    for k in range(1, groups):
        reduced = reduced + req_shift(down[k], groups - k)
    result = mixed + reduced
    states = result.astype(jnp.bfloat16).reshape(req_count, steps, width)
    return (
        states[:short_count],
        states[short_count:],
        key_now[:short_count],
        value_now[:short_count],
        key_now[short_count:],
        value_now[short_count:],
    )


def solution(mesh):
    in_specs = (
        P(("req", "seq"), None, None),
        P("req", None, None),
        P(("req", "seq"), None, None),
        P(("req", "seq"), None, None),
        P("req", "seq", None),
        P("req", "seq", None),
        P(("req", "seq")),
        P("req"),
        P(),
        P(),
        P(None, "req"),
        P(None, "req"),
        P(None, "req"),
        P("req", None),
        P(None, "req"),
        P("req", None),
    )
    out_specs = (
        P(("req", "seq"), None, None),
        P("req", None, None),
        P(("req", "seq"), None, None),
        P(("req", "seq"), None, None),
        P("req", None, None),
        P("req", None, None),
    )
    return jax.shard_map(shards, mesh=mesh, in_specs=in_specs, out_specs=out_specs, check_vma=False)
```

```python
import jax
import jax.numpy as jnp
from jax import lax
from jax.sharding import PartitionSpec as P

H = 16
HD = 64


masked_score = -1e30


def layer_norm(rows, gain):
    mean = jnp.mean(rows, axis=-1, keepdims=True)
    centred = rows - mean
    spread = jnp.mean(centred * centred, axis=-1, keepdims=True)
    return centred * lax.rsqrt(spread + 1e-05) * gain


def partial_block(query, keys, values, valid):
    scores = jnp.einsum("rthd,rphd->rthp", query, keys, preferred_element_type=jnp.float32) * 0.125
    scores = jnp.where(valid, scores, masked_score)
    peak = jnp.max(scores, axis=-1)
    weights = jnp.where(valid, jnp.exp(scores - peak[..., None]), 0.0)
    total = jnp.sum(weights, axis=-1)
    output = jnp.einsum(
        "rthp,rphd->rthd", weights.astype(jnp.bfloat16), values, preferred_element_type=jnp.float32
    )
    return (peak, total, output)


def cache_block(query, keys, values, valid):
    reqs, steps = query.shape[0], query.shape[1]
    eye = jnp.eye(H, dtype=query.dtype)
    spread = (query[:, :, :, None, :] * eye[None, None, :, :, None]).reshape(reqs, steps * H, H * HD)
    scores = jnp.einsum("rnc,rpc->rnp", spread, keys, preferred_element_type=jnp.float32) * 0.125
    scores = jnp.where(valid, scores, masked_score)
    peak = jnp.max(scores, axis=-1)
    weights = jnp.where(valid, jnp.exp(scores - peak[..., None]), 0.0)
    total = jnp.sum(weights, axis=-1)
    full = jnp.einsum(
        "rnp,rpc->rnc", weights.astype(jnp.bfloat16), values, preferred_element_type=jnp.float32
    ).reshape(reqs, steps, H, H, HD)
    output = jnp.sum(full * eye.astype(jnp.float32)[None, None, :, :, None], axis=3)
    return (peak.reshape(reqs, steps, H), total.reshape(reqs, steps, H), output)


def join(first, second):
    peak = jnp.maximum(first[0], second[0])
    scale_one = jnp.exp(first[0] - peak)
    scale_two = jnp.exp(second[0] - peak)
    total = first[1] * scale_one + second[1] * scale_two
    output = first[2] * scale_one[..., None] + second[2] * scale_two[..., None]
    return (peak, total, output)


def combine(parts, width):
    top = parts[0][:, width:width + 1]
    for part in parts[1:]:
        top = jnp.maximum(top, part[:, width:width + 1])
    merged = None
    for part in parts:
        scaled = part * jnp.exp(part[:, width:width + 1] - top)
        merged = scaled if merged is None else merged + scaled
    lanes = lax.broadcasted_iota(jnp.int32, merged.shape, 1)
    return jnp.where(lanes == width, top, merged)


def group_round_body(packed, size, stride, width):
    me = lax.axis_index("seq")
    total = lax.axis_size("seq")
    digit = (me // stride) % size
    received = [packed]
    for shift in range(1, size):
        pairs = []
        for i in range(total):
            e = (i // stride) % size
            pairs.append((i, i + ((e - shift) % size - e) * stride))
        received.append(lax.ppermute(packed, "seq", pairs))
    stacked = jnp.roll(jnp.stack(received), digit, axis=0)
    return combine([stacked[m] for m in range(size)], width)


def merge_long(partial_value):
    peak, total, output = partial_value
    shape = output.shape
    width = shape[-1]
    flat = output.reshape(-1, width)
    lanes = max(128, ((width + 2 + 127) // 128) * 128)
    packed = jnp.concatenate(
        [
            flat,
            peak.reshape(-1, 1),
            total.reshape(-1, 1),
            jnp.zeros((flat.shape[0], lanes - width - 2), flat.dtype),
        ],
        -1,
    )
    size = lax.axis_size("seq")
    stride = 1
    for radix in (2, 2, 2, 2, 2):
        if stride * radix > size or size % (stride * radix):
            break
        packed = group_round_body(packed, radix, stride, width)
        stride *= radix
    while stride < size:
        packed = group_round_body(packed, 2, stride, width)
        stride *= 2
    return (
        packed[:, width].reshape(shape[:-1]),
        packed[:, width + 1].reshape(shape[:-1]),
        packed[:, :width].reshape(shape),
    )


def req_shift(x, shift):
    n = lax.axis_size("req")
    return lax.ppermute(x, "req", [(i, (i - shift) % n) for i in range(n)])


def shards(
    short_tokens,
    long_tokens,
    short_keys,
    short_values,
    long_keys,
    long_values,
    short_lengths,
    long_lengths,
    attn_gain,
    ffn_gain,
    w_query,
    w_key,
    w_value,
    w_out,
    w_up,
    w_down,
):
    short_count = short_tokens.shape[0]
    long_count = long_tokens.shape[0]
    steps = short_tokens.shape[1]
    width = short_tokens.shape[2]
    req_count = short_count + long_count
    rows_count = req_count * steps
    groups = lax.axis_size("req")
    block = long_keys.shape[1]
    anchor = lax.axis_index("seq") * block
    short_valid = (jnp.arange(short_keys.shape[1])[None, :] < short_lengths[:, None])[:, None, :]
    long_valid = ((anchor + jnp.arange(block))[None, :] < long_lengths[:, None])[:, None, :]
    stacked = jnp.concatenate([w_query, w_key, w_value], 1)
    local = w_query.shape[1]
    fresh_ids = jnp.arange(steps)
    fresh_valid = (fresh_ids[None, :] <= fresh_ids[:, None])[None, :, None, :]

    rows = jnp.concatenate([short_tokens, long_tokens], 0).reshape(rows_count, width).astype(jnp.float32)
    normed = layer_norm(rows, attn_gain).astype(jnp.bfloat16)
    me = lax.axis_index("req")
    gathered = jnp.concatenate([normed] + [req_shift(normed, k) for k in range(1, groups)], 0)
    project_spread = jnp.dot(gathered, stacked, preferred_element_type=jnp.float32).astype(jnp.bfloat16)
    chunks = project_spread.reshape(groups, rows_count, 3 * local)
    returned = jnp.stack([chunks[0]] + [req_shift(chunks[groups - j], j) for j in range(1, groups)])
    moved = jnp.roll(returned, me, axis=0).transpose(1, 0, 2)
    moved = moved.reshape(rows_count, groups, 3, local)
    w_out, moved = lax.optimization_barrier((w_out, moved))
    w_out_parts = jnp.concatenate(
        [w_out] + [req_shift(w_out, k) for k in range(1, groups)], 0
    )
    query = moved[:, :, 0].reshape(req_count, steps, H, HD)
    key_now = moved[:, :, 1].reshape(req_count, steps, width)
    value_now = moved[:, :, 2].reshape(req_count, steps, width)
    fresh_k = key_now.reshape(req_count, steps, H, HD)
    fresh_v = value_now.reshape(req_count, steps, H, HD)
    long_raw = cache_block(query[short_count:], long_keys, long_values, long_valid)
    long_raw, query, fresh_k, fresh_v = lax.optimization_barrier((long_raw, query, fresh_k, fresh_v))
    long_part = merge_long(long_raw)
    fresh = partial_block(query, fresh_k, fresh_v, fresh_valid)
    short_part = cache_block(query[:short_count], short_keys, short_values, short_valid)
    cache_part = jax.tree.map(
        lambda first, second: jnp.concatenate([first, second], 0), short_part, long_part
    )
    _, total, output = join(cache_part, fresh)
    attended = output / total[..., None]
    attended = attended.reshape(rows_count, groups, width // groups).astype(jnp.bfloat16)
    attended = jnp.roll(attended, -me, axis=1).reshape(rows_count, width)
    mixed = rows + jnp.dot(attended, w_out_parts, preferred_element_type=jnp.float32)
    normed_ffn = layer_norm(mixed, ffn_gain).astype(jnp.bfloat16)
    gathered_ffn = jnp.concatenate(
        [normed_ffn] + [req_shift(normed_ffn, k) for k in range(1, groups)], 0
    )
    hidden = jax.nn.gelu(
        jnp.dot(gathered_ffn, w_up, preferred_element_type=jnp.float32),
        approximate=False,
    ).astype(jnp.bfloat16)
    down = jnp.dot(hidden, w_down, preferred_element_type=jnp.float32).reshape(groups, rows_count, width)
    reduced = down[0]
    for k in range(1, groups):
        reduced = reduced + req_shift(down[k], groups - k)
    cut = short_count * steps
    short_states = (mixed[:cut] + reduced[:cut]).astype(jnp.bfloat16)
    long_states = (mixed[cut:] + reduced[cut:]).astype(jnp.bfloat16)
    return (
        short_states.reshape(short_count, steps, width),
        long_states.reshape(long_count, steps, width),
        key_now[:short_count],
        value_now[:short_count],
        key_now[short_count:],
        value_now[short_count:],
    )


def solution(mesh):
    in_specs = (
        P(("req", "seq"), None, None),
        P("req", None, None),
        P(("req", "seq"), None, None),
        P(("req", "seq"), None, None),
        P("req", "seq", None),
        P("req", "seq", None),
        P(("req", "seq")),
        P("req"),
        P(),
        P(),
        P(None, "req"),
        P(None, "req"),
        P(None, "req"),
        P("req", None),
        P(None, "req"),
        P("req", None),
    )
    out_specs = (
        P(("req", "seq"), None, None),
        P("req", None, None),
        P(("req", "seq"), None, None),
        P(("req", "seq"), None, None),
        P("req", None, None),
        P("req", None, None),
    )
    return jax.shard_map(shards, mesh=mesh, in_specs=in_specs, out_specs=out_specs, check_vma=False)
```

```python
import jax
import jax.numpy as jnp
from jax import lax
from jax.sharding import PartitionSpec as P

H = 16
HD = 64


masked_score = -1e30


def layer_norm(rows, gain):
    mean = jnp.mean(rows, axis=-1, keepdims=True)
    centred = rows - mean
    spread = jnp.mean(centred * centred, axis=-1, keepdims=True)
    return centred * lax.rsqrt(spread + 1e-05) * gain


def spread_query(query):
    reqs, steps, width = query.shape
    head_of = lax.broadcasted_iota(jnp.int32, (H, width), 1) // HD
    mask = (head_of == lax.broadcasted_iota(jnp.int32, (H, width), 0)).astype(query.dtype)
    return (query[:, :, None, :] * mask[None, None, :, :]).reshape(reqs, steps * H, width)


def full_block(spread, keys, values, valid):
    scores = jnp.einsum("rnc,rpc->rnp", spread, keys, preferred_element_type=jnp.float32) * 0.125
    scores = jnp.where(valid, scores, masked_score)
    peak = jnp.max(scores, axis=-1)
    weights = jnp.where(valid, jnp.exp(scores - peak[..., None]), 0.0)
    total = jnp.sum(weights, axis=-1)
    full = jnp.einsum(
        "rnp,rpc->rnc", weights.astype(jnp.bfloat16), values, preferred_element_type=jnp.float32
    )
    return (peak, total, full)


def own_head(full):
    _, rows, width = full.shape
    row_head = lax.broadcasted_iota(jnp.int32, (rows, width), 0) % H
    lane_head = lax.broadcasted_iota(jnp.int32, (rows, width), 1) // HD
    picked = jnp.where((row_head == lane_head)[None], full, 0.0)
    select = (
        lax.broadcasted_iota(jnp.int32, (width, HD), 0) % HD
        == lax.broadcasted_iota(jnp.int32, (width, HD), 1)
    ).astype(jnp.float32)
    return jnp.einsum(
        "rnc,cd->rnd", picked, select, precision=lax.Precision.HIGHEST,
        preferred_element_type=jnp.float32,
    )


def join(first, second):
    peak = jnp.maximum(first[0], second[0])
    scale_one = jnp.exp(first[0] - peak)
    scale_two = jnp.exp(second[0] - peak)
    total = first[1] * scale_one + second[1] * scale_two
    output = first[2] * scale_one[..., None] + second[2] * scale_two[..., None]
    return (peak, total, output)


def combine(parts, width):
    top = parts[0][:, width:width + 1]
    for part in parts[1:]:
        top = jnp.maximum(top, part[:, width:width + 1])
    merged = None
    for part in parts:
        scaled = part * jnp.exp(part[:, width:width + 1] - top)
        merged = scaled if merged is None else merged + scaled
    lanes = lax.broadcasted_iota(jnp.int32, merged.shape, 1)
    return jnp.where(lanes == width, top, merged)


def group_round_body(packed, size, stride, width):
    me = lax.axis_index("seq")
    total = lax.axis_size("seq")
    digit = (me // stride) % size
    received = [packed]
    for shift in range(1, size):
        pairs = []
        for i in range(total):
            e = (i // stride) % size
            pairs.append((i, i + ((e - shift) % size - e) * stride))
        received.append(lax.ppermute(packed, "seq", pairs))
    stacked = jnp.roll(jnp.stack(received), digit, axis=0)
    return combine([stacked[m] for m in range(size)], width)


def merge_long(partial_value):
    peak, total, output = partial_value
    shape = output.shape
    width = shape[-1]
    flat = output.reshape(-1, width)
    lanes = max(128, ((width + 2 + 127) // 128) * 128)
    packed = jnp.concatenate(
        [
            flat,
            peak.reshape(-1, 1),
            total.reshape(-1, 1),
            jnp.zeros((flat.shape[0], lanes - width - 2), flat.dtype),
        ],
        -1,
    )
    size = lax.axis_size("seq")
    stride = 1
    for radix in (2, 4, 4):
        if stride * radix > size or size % (stride * radix):
            break
        packed = group_round_body(packed, radix, stride, width)
        stride *= radix
    while stride < size:
        packed = group_round_body(packed, 2, stride, width)
        stride *= 2
    return (
        packed[:, width].reshape(shape[:-1]),
        packed[:, width + 1].reshape(shape[:-1]),
        packed[:, :width].reshape(shape),
    )


def req_shift(x, shift):
    n = lax.axis_size("req")
    return lax.ppermute(x, "req", [(i, (i - shift) % n) for i in range(n)])


def shards(
    short_tokens,
    long_tokens,
    short_keys,
    short_values,
    long_keys,
    long_values,
    short_lengths,
    long_lengths,
    attn_gain,
    ffn_gain,
    w_query,
    w_key,
    w_value,
    w_out,
    w_up,
    w_down,
):
    short_count = short_tokens.shape[0]
    long_count = long_tokens.shape[0]
    steps = short_tokens.shape[1]
    width = short_tokens.shape[2]
    req_count = short_count + long_count
    rows_count = req_count * steps
    groups = lax.axis_size("req")
    block = long_keys.shape[1]
    anchor = lax.axis_index("seq") * block
    short_valid = (jnp.arange(short_keys.shape[1])[None, :] < short_lengths[:, None])[:, None, :]
    long_valid = ((anchor + jnp.arange(block))[None, :] < long_lengths[:, None])[:, None, :]
    stacked = jnp.concatenate([w_query, w_key, w_value], 1)
    local = w_query.shape[1]
    fresh_ids = jnp.arange(steps)
    fresh_valid = jnp.repeat(fresh_ids[None, :] <= fresh_ids[:, None], H, axis=0)[None]

    rows = jnp.concatenate([short_tokens, long_tokens], 0).reshape(rows_count, width).astype(jnp.float32)
    normed = layer_norm(rows, attn_gain).astype(jnp.bfloat16)
    me = lax.axis_index("req")
    gathered = jnp.concatenate([normed] + [req_shift(normed, k) for k in range(1, groups)], 0)
    project_spread = jnp.dot(gathered, stacked, preferred_element_type=jnp.float32).astype(jnp.bfloat16)
    chunks = project_spread.reshape(groups, rows_count, 3 * local)
    returned = jnp.stack([chunks[0]] + [req_shift(chunks[groups - j], j) for j in range(1, groups)])
    moved = jnp.roll(returned, me, axis=0).transpose(1, 0, 2)
    moved = moved.reshape(rows_count, groups, 3, local)
    w_out, moved = lax.optimization_barrier((w_out, moved))
    w_out_parts = jnp.concatenate(
        [w_out] + [req_shift(w_out, k) for k in range(1, groups)], 0
    )
    query = moved[:, :, 0].reshape(req_count, steps, width)
    key_now = moved[:, :, 1].reshape(req_count, steps, width)
    value_now = moved[:, :, 2].reshape(req_count, steps, width)
    spread = spread_query(query)
    long_peak, long_total, long_full = full_block(
        spread[short_count:], long_keys, long_values, long_valid
    )
    long_raw = (long_peak, long_total, own_head(long_full))
    long_raw, spread, key_now, value_now = lax.optimization_barrier(
        (long_raw, spread, key_now, value_now)
    )
    long_part = merge_long(long_raw)
    fresh = full_block(spread, key_now, value_now, fresh_valid)
    short_cache = full_block(spread[:short_count], short_keys, short_values, short_valid)
    short_fresh = jax.tree.map(lambda part: part[:short_count], fresh)
    _, short_total, short_full = join(short_cache, short_fresh)
    long_fresh = jax.tree.map(lambda part: part[short_count:], fresh)
    picked = own_head(jnp.concatenate([short_full, long_fresh[2]], 0))
    long_peak, long_total, long_out = join(
        long_part, (long_fresh[0], long_fresh[1], picked[short_count:])
    )
    total = jnp.concatenate([short_total, long_total], 0)
    output = jnp.concatenate([picked[:short_count], long_out], 0)
    attended = output / total[..., None]
    attended = attended.reshape(rows_count, groups, width // groups).astype(jnp.bfloat16)
    attended = jnp.roll(attended, -me, axis=1).reshape(rows_count, width)
    mixed = rows + jnp.dot(attended, w_out_parts, preferred_element_type=jnp.float32)
    normed_ffn = layer_norm(mixed, ffn_gain).astype(jnp.bfloat16)
    gathered_ffn = jnp.concatenate(
        [normed_ffn] + [req_shift(normed_ffn, k) for k in range(1, groups)], 0
    )
    hidden = jax.nn.gelu(
        jnp.dot(gathered_ffn, w_up, preferred_element_type=jnp.float32),
        approximate=False,
    ).astype(jnp.bfloat16)
    down = jnp.dot(hidden, w_down, preferred_element_type=jnp.float32).reshape(groups, rows_count, width)
    reduced = down[0]
    for k in range(1, groups):
        reduced = reduced + req_shift(down[k], groups - k)
    cut = short_count * steps
    short_states = (mixed[:cut] + reduced[:cut]).astype(jnp.bfloat16)
    long_states = (mixed[cut:] + reduced[cut:]).astype(jnp.bfloat16)
    return (
        short_states.reshape(short_count, steps, width),
        long_states.reshape(long_count, steps, width),
        key_now[:short_count],
        value_now[:short_count],
        key_now[short_count:],
        value_now[short_count:],
    )


def solution(mesh):
    in_specs = (
        P(("req", "seq"), None, None),
        P("req", None, None),
        P(("req", "seq"), None, None),
        P(("req", "seq"), None, None),
        P("req", "seq", None),
        P("req", "seq", None),
        P(("req", "seq")),
        P("req"),
        P(),
        P(),
        P(None, "req"),
        P(None, "req"),
        P(None, "req"),
        P("req", None),
        P(None, "req"),
        P("req", None),
    )
    out_specs = (
        P(("req", "seq"), None, None),
        P("req", None, None),
        P(("req", "seq"), None, None),
        P(("req", "seq"), None, None),
        P("req", None, None),
        P("req", None, None),
    )
    return jax.shard_map(shards, mesh=mesh, in_specs=in_specs, out_specs=out_specs, check_vma=False)
```

```python
import jax
import jax.numpy as jnp
from jax import lax
from jax.sharding import PartitionSpec as P

H = 16
HD = 64


masked_score = -1e30


def layer_norm(rows, gain):
    mean = jnp.mean(rows, axis=-1, keepdims=True)
    centred = rows - mean
    spread = jnp.mean(centred * centred, axis=-1, keepdims=True)
    return centred * lax.rsqrt(spread + 1e-05) * gain


def spread_query(query):
    reqs, steps, width = query.shape
    head_of = lax.broadcasted_iota(jnp.int32, (H, width), 1) // HD
    mask = (head_of == lax.broadcasted_iota(jnp.int32, (H, width), 0)).astype(query.dtype)
    return (query[:, :, None, :] * mask[None, None, :, :]).reshape(reqs, steps * H, width)


def full_block(spread, keys, values, valid):
    scores = jnp.einsum("rnc,rpc->rnp", spread, keys, preferred_element_type=jnp.float32) * 0.125
    scores = jnp.where(valid, scores, masked_score)
    peak = jnp.max(scores, axis=-1)
    weights = jnp.where(valid, jnp.exp(scores - peak[..., None]), 0.0)
    total = jnp.sum(weights, axis=-1)
    full = jnp.einsum(
        "rnp,rpc->rnc", weights.astype(jnp.bfloat16), values, preferred_element_type=jnp.float32
    )
    return (peak, total, full)


def own_head(full):
    _, rows, width = full.shape
    row_head = lax.broadcasted_iota(jnp.int32, (rows, width), 0) % H
    lane_head = lax.broadcasted_iota(jnp.int32, (rows, width), 1) // HD
    picked = jnp.where((row_head == lane_head)[None], full, 0.0)
    select = (
        lax.broadcasted_iota(jnp.int32, (width, HD), 0) % HD
        == lax.broadcasted_iota(jnp.int32, (width, HD), 1)
    ).astype(jnp.float32)
    return jnp.einsum(
        "rnc,cd->rnd", picked, select, precision=lax.Precision.HIGHEST,
        preferred_element_type=jnp.float32,
    )


def join(first, second):
    peak = jnp.maximum(first[0], second[0])
    scale_one = jnp.exp(first[0] - peak)
    scale_two = jnp.exp(second[0] - peak)
    total = first[1] * scale_one + second[1] * scale_two
    output = first[2] * scale_one[..., None] + second[2] * scale_two[..., None]
    return (peak, total, output)


def combine(parts, width):
    top = parts[0][:, width:width + 1]
    for part in parts[1:]:
        top = jnp.maximum(top, part[:, width:width + 1])
    merged = None
    for part in parts:
        scaled = part * jnp.exp(part[:, width:width + 1] - top)
        merged = scaled if merged is None else merged + scaled
    lanes = lax.broadcasted_iota(jnp.int32, merged.shape, 1)
    return jnp.where(lanes == width, top, merged)


def group_round_body(packed, size, stride, width):
    me = lax.axis_index("seq")
    total = lax.axis_size("seq")
    digit = (me // stride) % size
    received = [packed]
    for shift in range(1, size):
        pairs = []
        for i in range(total):
            e = (i // stride) % size
            pairs.append((i, i + ((e - shift) % size - e) * stride))
        received.append(lax.ppermute(packed, "seq", pairs))
    stacked = jnp.roll(jnp.stack(received), digit, axis=0)
    return combine([stacked[m] for m in range(size)], width)


def merge_long(partial_value):
    peak, total, output = partial_value
    shape = output.shape
    width = shape[-1]
    flat = output.reshape(-1, width)
    lanes = max(128, ((width + 2 + 127) // 128) * 128)
    packed = jnp.concatenate(
        [
            flat,
            peak.reshape(-1, 1),
            total.reshape(-1, 1),
            jnp.zeros((flat.shape[0], lanes - width - 2), flat.dtype),
        ],
        -1,
    )
    size = lax.axis_size("seq")
    stride = 1
    for radix in (2, 4, 4):
        if stride * radix > size or size % (stride * radix):
            break
        packed = group_round_body(packed, radix, stride, width)
        stride *= radix
    while stride < size:
        packed = group_round_body(packed, 2, stride, width)
        stride *= 2
    return (
        packed[:, width].reshape(shape[:-1]),
        packed[:, width + 1].reshape(shape[:-1]),
        packed[:, :width].reshape(shape),
    )


def req_shift(x, shift):
    n = lax.axis_size("req")
    return lax.ppermute(x, "req", [(i, (i - shift) % n) for i in range(n)])


def shards(
    short_tokens,
    long_tokens,
    short_keys,
    short_values,
    long_keys,
    long_values,
    short_lengths,
    long_lengths,
    attn_gain,
    ffn_gain,
    w_query,
    w_key,
    w_value,
    w_out,
    w_up,
    w_down,
):
    short_count = short_tokens.shape[0]
    long_count = long_tokens.shape[0]
    steps = short_tokens.shape[1]
    width = short_tokens.shape[2]
    req_count = short_count + long_count
    rows_count = req_count * steps
    groups = lax.axis_size("req")
    block = long_keys.shape[1]
    anchor = lax.axis_index("seq") * block
    short_valid = (jnp.arange(short_keys.shape[1])[None, :] < short_lengths[:, None])[:, None, :]
    long_valid = ((anchor + jnp.arange(block))[None, :] < long_lengths[:, None])[:, None, :]
    stacked = jnp.concatenate([w_query, w_key, w_value], 1)
    local = w_query.shape[1]
    fresh_ids = jnp.arange(steps)
    fresh_valid = jnp.repeat(fresh_ids[None, :] <= fresh_ids[:, None], H, axis=0)[None]

    rows = jnp.concatenate([short_tokens, long_tokens], 0).reshape(rows_count, width).astype(jnp.float32)
    normed = layer_norm(rows, attn_gain).astype(jnp.bfloat16)
    me = lax.axis_index("req")
    gathered = jnp.concatenate([normed] + [req_shift(normed, k) for k in range(1, groups)], 0)
    project_spread = jnp.dot(gathered, stacked, preferred_element_type=jnp.float32).astype(jnp.bfloat16)
    chunks = project_spread.reshape(groups, rows_count, 3 * local)
    returned = jnp.stack([chunks[0]] + [req_shift(chunks[groups - j], j) for j in range(1, groups)])
    moved = jnp.roll(returned, me, axis=0).transpose(1, 0, 2)
    moved = moved.reshape(rows_count, groups, 3, local)
    w_out_parts = jnp.concatenate(
        [w_out] + [req_shift(w_out, k) for k in range(1, groups)], 0
    )
    query = moved[:, :, 0].reshape(req_count, steps, width)
    key_now = moved[:, :, 1].reshape(req_count, steps, width)
    value_now = moved[:, :, 2].reshape(req_count, steps, width)
    spread = spread_query(query)
    long_peak, long_total, long_full = full_block(
        spread[short_count:], long_keys, long_values, long_valid
    )
    long_raw = (long_peak, long_total, own_head(long_full))
    long_raw, spread, key_now, value_now = lax.optimization_barrier(
        (long_raw, spread, key_now, value_now)
    )
    long_part = merge_long(long_raw)
    fresh = full_block(spread, key_now, value_now, fresh_valid)
    short_cache = full_block(spread[:short_count], short_keys, short_values, short_valid)
    short_fresh = jax.tree.map(lambda part: part[:short_count], fresh)
    _, short_total, short_full = join(short_cache, short_fresh)
    long_fresh = jax.tree.map(lambda part: part[short_count:], fresh)
    picked = own_head(jnp.concatenate([short_full, long_fresh[2]], 0))
    short_total, picked, fresh_peak, fresh_total = lax.optimization_barrier(
        (short_total, picked, long_fresh[0], long_fresh[1])
    )
    long_peak, long_total, long_out = join(
        long_part, (fresh_peak, fresh_total, picked[short_count:])
    )
    total = jnp.concatenate([short_total, long_total], 0)
    output = jnp.concatenate([picked[:short_count], long_out], 0)
    attended = output / total[..., None]
    attended = attended.reshape(rows_count, groups, width // groups).astype(jnp.bfloat16)
    attended = jnp.roll(attended, -me, axis=1).reshape(rows_count, width)
    mixed = rows + jnp.dot(attended, w_out_parts, preferred_element_type=jnp.float32)
    normed_ffn = layer_norm(mixed, ffn_gain).astype(jnp.bfloat16)
    gathered_ffn = jnp.concatenate(
        [normed_ffn] + [req_shift(normed_ffn, k) for k in range(1, groups)], 0
    )
    hidden = jax.nn.gelu(
        jnp.dot(gathered_ffn, w_up, preferred_element_type=jnp.float32),
        approximate=False,
    ).astype(jnp.bfloat16)
    down = jnp.dot(hidden, w_down, preferred_element_type=jnp.float32).reshape(groups, rows_count, width)
    reduced = down[0]
    for k in range(1, groups):
        reduced = reduced + req_shift(down[k], groups - k)
    cut = short_count * steps
    short_states = (mixed[:cut] + reduced[:cut]).astype(jnp.bfloat16)
    long_states = (mixed[cut:] + reduced[cut:]).astype(jnp.bfloat16)
    return (
        short_states.reshape(short_count, steps, width),
        long_states.reshape(long_count, steps, width),
        key_now[:short_count],
        value_now[:short_count],
        key_now[short_count:],
        value_now[short_count:],
    )


def solution(mesh):
    in_specs = (
        P(("req", "seq"), None, None),
        P("req", None, None),
        P(("req", "seq"), None, None),
        P(("req", "seq"), None, None),
        P("req", "seq", None),
        P("req", "seq", None),
        P(("req", "seq")),
        P("req"),
        P(),
        P(),
        P(None, "req"),
        P(None, "req"),
        P(None, "req"),
        P("req", None),
        P(None, "req"),
        P("req", None),
    )
    out_specs = (
        P(("req", "seq"), None, None),
        P("req", None, None),
        P(("req", "seq"), None, None),
        P(("req", "seq"), None, None),
        P("req", None, None),
        P("req", None, None),
    )
    return jax.shard_map(shards, mesh=mesh, in_specs=in_specs, out_specs=out_specs, check_vma=False)
```

```python
import jax
import jax.numpy as jnp
from jax import lax
from jax.sharding import PartitionSpec as P

H = 16
HD = 64


masked_score = -1e30


def layer_norm(rows, gain):
    mean = jnp.mean(rows, axis=-1, keepdims=True)
    centred = rows - mean
    spread = jnp.mean(centred * centred, axis=-1, keepdims=True)
    return centred * lax.rsqrt(spread + 1e-05) * gain


def spread_query(query):
    reqs, steps, width = query.shape
    head_of = lax.broadcasted_iota(jnp.int32, (H, width), 1) // HD
    mask = (head_of == lax.broadcasted_iota(jnp.int32, (H, width), 0)).astype(query.dtype)
    return (query[:, :, None, :] * mask[None, None, :, :]).reshape(reqs, steps * H, width)


def full_block(spread, keys, values, valid):
    scores = jnp.einsum("rnc,rpc->rnp", spread, keys, preferred_element_type=jnp.float32) * 0.125
    scores = jnp.where(valid, scores, masked_score)
    peak = jnp.max(scores, axis=-1)
    weights = jnp.where(valid, jnp.exp(scores - peak[..., None]), 0.0)
    total = jnp.sum(weights, axis=-1)
    full = jnp.einsum(
        "rnp,rpc->rnc", weights.astype(jnp.bfloat16), values, preferred_element_type=jnp.float32
    )
    return (peak, total, full)


def own_head(full):
    _, rows, width = full.shape
    row_head = lax.broadcasted_iota(jnp.int32, (rows, width), 0) % H
    lane_head = lax.broadcasted_iota(jnp.int32, (rows, width), 1) // HD
    picked = jnp.where((row_head == lane_head)[None], full, 0.0)
    select = (
        lax.broadcasted_iota(jnp.int32, (width, HD), 0) % HD
        == lax.broadcasted_iota(jnp.int32, (width, HD), 1)
    ).astype(jnp.float32)
    return jnp.einsum(
        "rnc,cd->rnd", picked, select, precision=lax.Precision.HIGHEST,
        preferred_element_type=jnp.float32,
    )


def join(first, second):
    peak = jnp.maximum(first[0], second[0])
    scale_one = jnp.exp(first[0] - peak)
    scale_two = jnp.exp(second[0] - peak)
    total = first[1] * scale_one + second[1] * scale_two
    output = first[2] * scale_one[..., None] + second[2] * scale_two[..., None]
    return (peak, total, output)


def combine(parts, width):
    top = parts[0][width:width + 1]
    for part in parts[1:]:
        top = jnp.maximum(top, part[width:width + 1])
    merged = None
    for part in parts:
        scaled = part * jnp.exp(part[width:width + 1] - top)
        merged = scaled if merged is None else merged + scaled
    feature = lax.broadcasted_iota(jnp.int32, merged.shape, 0)
    return jnp.where(feature == width, top, merged)


def group_round_body(packed, size, stride, width):
    me = lax.axis_index("seq")
    total = lax.axis_size("seq")
    digit = (me // stride) % size
    received = [packed]
    for shift in range(1, size):
        pairs = []
        for i in range(total):
            e = (i // stride) % size
            pairs.append((i, i + ((e - shift) % size - e) * stride))
        received.append(lax.ppermute(packed, "seq", pairs))
    stacked = jnp.roll(jnp.stack(received), digit, axis=0)
    return combine([stacked[m] for m in range(size)], width)


def merge_long(partial_value):
    peak, total, output = partial_value
    shape = output.shape
    width = shape[-1]
    flat = output.reshape(-1, width)
    pad = (-(width + 2)) % 8
    packed = jnp.concatenate(
        [
            flat.T,
            peak.reshape(1, -1),
            total.reshape(1, -1),
            jnp.zeros((pad, flat.shape[0]), flat.dtype),
        ],
        0,
    )
    size = lax.axis_size("seq")
    stride = 1
    for radix in (2, 4, 4):
        if stride * radix > size or size % (stride * radix):
            break
        packed = group_round_body(packed, radix, stride, width)
        stride *= radix
    while stride < size:
        packed = group_round_body(packed, 2, stride, width)
        stride *= 2
    return (
        packed[width].reshape(shape[:-1]),
        packed[width + 1].reshape(shape[:-1]),
        packed[:width].T.reshape(shape),
    )


def req_shift(x, shift):
    n = lax.axis_size("req")
    return lax.ppermute(x, "req", [(i, (i - shift) % n) for i in range(n)])


def shards(
    short_tokens,
    long_tokens,
    short_keys,
    short_values,
    long_keys,
    long_values,
    short_lengths,
    long_lengths,
    attn_gain,
    ffn_gain,
    w_query,
    w_key,
    w_value,
    w_out,
    w_up,
    w_down,
):
    short_count = short_tokens.shape[0]
    long_count = long_tokens.shape[0]
    steps = short_tokens.shape[1]
    width = short_tokens.shape[2]
    req_count = short_count + long_count
    rows_count = req_count * steps
    groups = lax.axis_size("req")
    block = long_keys.shape[1]
    anchor = lax.axis_index("seq") * block
    short_valid = (jnp.arange(short_keys.shape[1])[None, :] < short_lengths[:, None])[:, None, :]
    long_valid = ((anchor + jnp.arange(block))[None, :] < long_lengths[:, None])[:, None, :]
    stacked = jnp.concatenate([w_query, w_key, w_value], 1)
    local = w_query.shape[1]
    fresh_ids = jnp.arange(steps)
    fresh_valid = jnp.repeat(fresh_ids[None, :] <= fresh_ids[:, None], H, axis=0)[None]

    rows = jnp.concatenate([short_tokens, long_tokens], 0).reshape(rows_count, width).astype(jnp.float32)
    normed = layer_norm(rows, attn_gain).astype(jnp.bfloat16)
    me = lax.axis_index("req")
    gathered = jnp.concatenate([normed] + [req_shift(normed, k) for k in range(1, groups)], 0)
    project_spread = jnp.dot(gathered, stacked, preferred_element_type=jnp.float32).astype(jnp.bfloat16)
    chunks = project_spread.reshape(groups, rows_count, 3 * local)
    returned = jnp.stack([chunks[0]] + [req_shift(chunks[groups - j], j) for j in range(1, groups)])
    moved = jnp.roll(returned, me, axis=0).transpose(1, 0, 2)
    moved = moved.reshape(rows_count, groups, 3, local)
    w_out_parts = jnp.concatenate(
        [w_out] + [req_shift(w_out, k) for k in range(1, groups)], 0
    )
    query = moved[:, :, 0].reshape(req_count, steps, width)
    key_now = moved[:, :, 1].reshape(req_count, steps, width)
    value_now = moved[:, :, 2].reshape(req_count, steps, width)
    spread = spread_query(query)
    long_peak, long_total, long_full = full_block(
        spread[short_count:], long_keys, long_values, long_valid
    )
    long_raw = (long_peak, long_total, own_head(long_full))
    long_raw, spread, key_now, value_now = lax.optimization_barrier(
        (long_raw, spread, key_now, value_now)
    )
    long_part = merge_long(long_raw)
    fresh = full_block(spread, key_now, value_now, fresh_valid)
    short_cache = full_block(spread[:short_count], short_keys, short_values, short_valid)
    short_fresh = jax.tree.map(lambda part: part[:short_count], fresh)
    _, short_total, short_full = join(short_cache, short_fresh)
    long_fresh = jax.tree.map(lambda part: part[short_count:], fresh)
    picked = own_head(jnp.concatenate([short_full, long_fresh[2]], 0))
    short_total, picked, fresh_peak, fresh_total = lax.optimization_barrier(
        (short_total, picked, long_fresh[0], long_fresh[1])
    )
    long_peak, long_total, long_out = join(
        long_part, (fresh_peak, fresh_total, picked[short_count:])
    )
    total = jnp.concatenate([short_total, long_total], 0)
    output = jnp.concatenate([picked[:short_count], long_out], 0)
    attended = output / total[..., None]
    attended = attended.reshape(rows_count, groups, width // groups).astype(jnp.bfloat16)
    attended = jnp.roll(attended, -me, axis=1).reshape(rows_count, width)
    mixed = rows + jnp.dot(attended, w_out_parts, preferred_element_type=jnp.float32)
    normed_ffn = layer_norm(mixed, ffn_gain).astype(jnp.bfloat16)
    gathered_ffn = jnp.concatenate(
        [normed_ffn] + [req_shift(normed_ffn, k) for k in range(1, groups)], 0
    )
    hidden = jax.nn.gelu(
        jnp.dot(gathered_ffn, w_up, preferred_element_type=jnp.float32),
        approximate=False,
    ).astype(jnp.bfloat16)
    down = jnp.dot(hidden, w_down, preferred_element_type=jnp.float32).reshape(groups, rows_count, width)
    reduced = down[0]
    for k in range(1, groups):
        reduced = reduced + req_shift(down[k].astype(jnp.bfloat16), groups - k).astype(jnp.float32)
    cut = short_count * steps
    short_states = (mixed[:cut] + reduced[:cut]).astype(jnp.bfloat16)
    long_states = (mixed[cut:] + reduced[cut:]).astype(jnp.bfloat16)
    return (
        short_states.reshape(short_count, steps, width),
        long_states.reshape(long_count, steps, width),
        key_now[:short_count],
        value_now[:short_count],
        key_now[short_count:],
        value_now[short_count:],
    )


def solution(mesh):
    in_specs = (
        P(("req", "seq"), None, None),
        P("req", None, None),
        P(("req", "seq"), None, None),
        P(("req", "seq"), None, None),
        P("req", "seq", None),
        P("req", "seq", None),
        P(("req", "seq")),
        P("req"),
        P(),
        P(),
        P(None, "req"),
        P(None, "req"),
        P(None, "req"),
        P("req", None),
        P(None, "req"),
        P("req", None),
    )
    out_specs = (
        P(("req", "seq"), None, None),
        P("req", None, None),
        P(("req", "seq"), None, None),
        P(("req", "seq"), None, None),
        P("req", None, None),
        P("req", None, None),
    )
    return jax.shard_map(shards, mesh=mesh, in_specs=in_specs, out_specs=out_specs, check_vma=False)
```
